32 devices in a mesh: cuts: 2 (over y), dp: 2 (over x), row: 2 (over core), col: 4 (over z).
Axes of the slice: x: 2, y: 2, z: 4, core: 2. Of those that a mesh axis runs over, the one named last changes fastest.
Arguments:
- tokens: bfloat16 [4096, 4096], P(('cuts', 'dp'), 'row'), may hold values from -6 to 6
- cotangent: bfloat16 [4096, 4096], P(('cuts', 'dp'), 'col'), may hold values from -0.09375 to 0.09375
- norm_gain: float32 [4096], P('row'), may hold values from 0.5 to 6
- row_prev: float32 [2, 2048], P('row', 'dp'), may hold values from 0.02 to 0.5
- col_prev: float32 [4096], P('col'), may hold values from 0.002 to 0.05
Outputs:
- update: float32 [2, 2048, 4096], P('row', 'dp', 'col')
- row_moment: float32 [2, 2048], P('row', 'dp')
- col_moment: float32 [4096], P('col')
The draws below stay inside these ranges and needn't reach their ends.
All inputs are finite; a program needn't handle non-finite values.
Results may differ from the reference program's by a relative error of at most 0.0004.
Values sent between devices are 32-bit elements; how exact they have to be, the bound alone decides.
No kernel may reach another device: no remote copies, remote signals or barrier semaphores. Data moves between devices by JAX's collectives and lax.ppermute only.
A program may use at most 64 MiB of HBM per device.

```python
import math
import jax
import jax.numpy as jnp
from jax import lax

D = 4096
TOK_DEV = 1024
F = 4096
TOKENS = 4096
SLABS = 2
SLAB_ROWS = 2048
N_CUTS = 2
N_DP = 2


def draw_norm_gain(key, part):
    position = jnp.arange(D, dtype=jnp.float32) / (D - 1)
    trend = jnp.power(3.0, position)
    noise = jnp.exp(jax.random.uniform(key, (D,), jnp.float32, -0.69, 0.69))
    return trend * noise


def levels(stream_key, extent, pieces, least, high):
    gain = 1.0
    for axis_at, blocks in pieces:
        heights = jax.random.uniform(jax.random.fold_in(jax.random.fold_in(stream_key, 6), axis_at), (blocks,), jnp.float32, least / len(pieces), high / len(pieces))
        gain = gain * jnp.repeat(jnp.exp(heights), extent[axis_at] // blocks).reshape((-1,) + (1,) * (len(extent) - 1 - axis_at))
    return gain


def bell_draw(own_key, dims, width, reach, cuts=(), kind=jnp.bfloat16):
    result = jax.random.normal(own_key, dims, jnp.float32) * width
    if len(cuts) > 0:
        result = levels(own_key, dims, cuts, -0.22, 0.18) * result
    return jnp.clip(result, min=-reach, max=reach).astype(kind)


def setup_inputs(seed: int = 0) -> dict:
    arg_keys = jax.random.split(jax.random.key(seed), 6)
    return {
        "tokens": bell_draw(arg_keys[0], (TOKENS, D), 1.0, 6.0, ((0, 4), (1, 2))),
        "cotangent": bell_draw(arg_keys[1], (TOKENS, F), TOKENS ** -0.5, 0.09375, ((0, 4), (1, 4))),
        "norm_gain": draw_norm_gain(jax.random.fold_in(arg_keys[5], 71), 0),
        "row_prev": jnp.clip(jnp.exp(math.log(0.5) - 3.218876 * jax.random.uniform(arg_keys[3], (SLABS, SLAB_ROWS), jnp.float32) ** levels(arg_keys[3], (SLABS, SLAB_ROWS), ((0, 2), (1, 2)), -0.2, 0.2)), 0.02, 0.5),
        "col_prev": jnp.clip(jnp.exp(math.log(0.05) - 3.218876 * jax.random.uniform(arg_keys[4], (F,), jnp.float32) ** levels(arg_keys[4], (F,), ((0, 4),), -0.2, 0.2)), 0.002, 0.05),
    }


decay_rate = 0.975
epsilon_one = 1e-30
clip_level = 1.0

def reference(tokens, cotangent, norm_gain, row_prev, col_prev):
    groups_count = N_CUTS * N_DP
    token_groups = tokens.reshape(groups_count, TOK_DEV, D)
    cot_groups = cotangent.reshape(groups_count, TOK_DEV, F)
    gradient = jnp.zeros((D, F), jnp.float32)
    for group in range(groups_count):
        product = jnp.dot(token_groups[group].T, cot_groups[group], preferred_element_type=jnp.float32)
        gradient = gradient + product * norm_gain[:, None]
    squares = gradient * gradient
    rows_prev = row_prev.reshape(D)
    row_moment = decay_rate * rows_prev + (1.0 - decay_rate) * (lax.optimization_barrier(jnp.sum(squares, axis=1)) / F + epsilon_one)
    col_moment = decay_rate * col_prev + (1.0 - decay_rate) * (lax.optimization_barrier(jnp.sum(squares, axis=0)) / D + epsilon_one)
    factor = row_moment[:, None] * col_moment[None, :]
    raw_update = gradient / jnp.sqrt(factor)
    clip_scale = jnp.maximum(1.0, jnp.sqrt(jnp.sum(raw_update * raw_update) / (D * F)) / clip_level)
    update = (raw_update / clip_scale).reshape(SLABS, SLAB_ROWS, F)
    return (update, row_moment.reshape(SLABS, SLAB_ROWS), col_moment)
```

```python
import jax
import jax.numpy as jnp
from jax import lax
from jax.sharding import PartitionSpec as P

D = 4096
F = 4096


decay_rate = 0.975
epsilon_one = 1e-30
clip_level = 1.0

ALL_AXES = ("cuts", "dp", "row", "col")
SWAP = [(0, 1), (1, 0)]
CHUNKS = 4


def gradient_rows(inputs, cotangent, gains):
    product = lax.dot_general(
        inputs, cotangent, (((0,), (0,)), ((), ())), preferred_element_type=jnp.float32
    )
    return product * gains[:, None]


def adafactor_step(gradient, rows_prev, cols_prev, down_columns, all_total):
    squares = gradient * gradient
    row_sum = lax.psum(jnp.sum(squares, axis=1), "col")
    col_sum = down_columns(jnp.sum(squares, axis=0))
    row_moment = decay_rate * rows_prev + (1.0 - decay_rate) * (row_sum / F + epsilon_one)
    col_moment = decay_rate * cols_prev + (1.0 - decay_rate) * (col_sum / D + epsilon_one)
    factor = row_moment[:, None] * col_moment[None, :]
    raw_update = gradient / jnp.sqrt(factor)
    total_squares = all_total(jnp.sum(raw_update * raw_update))
    clip_scale = jnp.maximum(1.0, jnp.sqrt(total_squares / (D * F)) / clip_level)
    return (raw_update / clip_scale, row_moment, col_moment)


def body(tokens, cotangent, norm_gain, row_prev, col_prev):
    slice_part = lax.psum_scatter(
        gradient_rows(tokens, cotangent, norm_gain), "dp", scatter_dimension=0, tiled=True
    )
    gradient = lax.psum(slice_part, "cuts")
    update, row_moment, col_moment = adafactor_step(
        gradient,
        row_prev[0],
        col_prev,
        lambda values: lax.psum(values, ("dp", "row")),
        lambda values: lax.psum(values, ("dp", "row", "col")),
    )
    return (update[None], row_moment[None], col_moment)


def first_replica(values):
    return jnp.where(lax.axis_index("cuts") == 0, values, jnp.zeros_like(values))


def body_swap(tokens, cotangent, norm_gain, row_prev, col_prev):
    n_dp = lax.axis_size("dp")
    n_row = lax.axis_size("row")
    n_col = lax.axis_size("col")
    d = lax.axis_index("dp")
    r = lax.axis_index("row")
    k = lax.axis_index("col")
    rows = tokens.shape[1]
    half = rows // n_dp
    cols = cotangent.shape[1]
    width = cols // CHUNKS

    pieces = []
    for c in range(CHUNKS):
        part = gradient_rows(tokens, cotangent[:, c * width:(c + 1) * width], norm_gain)
        send = lax.dynamic_slice_in_dim(part, (1 - d) * half, half, axis=0)
        own = lax.dynamic_slice_in_dim(part, d * half, half, axis=0)
        slice_sum = own + lax.ppermute(send, "dp", SWAP)
        pieces.append(slice_sum + lax.ppermute(slice_sum, "cuts", SWAP))
    gradient = jnp.concatenate(pieces, axis=1)

    squares = gradient * gradient
    row_local = jnp.sum(squares, axis=1)
    col_local = jnp.sum(squares, axis=0)
    n_row_slots = n_row * n_dp * half
    slots = jnp.zeros((n_row_slots + n_col * cols,), jnp.float32)
    slots = lax.dynamic_update_slice(slots, row_local, ((r * n_dp + d) * half,))
    slots = lax.dynamic_update_slice(slots, col_local, (n_row_slots + k * cols,))
    slots = lax.psum(first_replica(slots), ALL_AXES)
    row_sum = lax.dynamic_slice_in_dim(slots, (r * n_dp + d) * half, half)
    col_sum = lax.dynamic_slice_in_dim(slots, n_row_slots + k * cols, cols)

    row_moment = decay_rate * row_prev[0] + (1.0 - decay_rate) * (row_sum / F + epsilon_one)
    col_moment = decay_rate * col_prev + (1.0 - decay_rate) * (col_sum / D + epsilon_one)
    factor = row_moment[:, None] * col_moment[None, :]
    raw_update = gradient / jnp.sqrt(factor)
    total_squares = lax.psum(first_replica(jnp.sum(raw_update * raw_update)), ALL_AXES)
    clip_scale = jnp.maximum(1.0, jnp.sqrt(total_squares / (D * F)) / clip_level)
    return ((raw_update / clip_scale)[None], row_moment[None], col_moment)


def solution(mesh):
    fast = mesh.shape["dp"] == 2 and mesh.shape["cuts"] == 2
    return jax.shard_map(
        body_swap if fast else body,
        mesh=mesh,
        in_specs=(
            P(("cuts", "dp"), "row"),
            P(("cuts", "dp"), "col"),
            P("row"),
            P("row", "dp"),
            P("col"),
        ),
        out_specs=(P("row", "dp", "col"), P("row", "dp"), P("col")),
        check_vma=False,
    )
```

```python
import jax
import jax.numpy as jnp
from jax import lax
from jax.sharding import PartitionSpec as P

D = 4096
F = 4096


decay_rate = 0.975
epsilon_one = 1e-30
clip_level = 1.0

SWAP = [(0, 1), (1, 0)]
CHUNKS = 8


def gradient_rows(inputs, cotangent, gains):
    product = lax.dot_general(
        inputs, cotangent, (((0,), (0,)), ((), ())), preferred_element_type=jnp.float32
    )
    return product * gains[:, None]


def adafactor_step(gradient, rows_prev, cols_prev, down_columns, all_total):
    squares = gradient * gradient
    row_sum = lax.psum(jnp.sum(squares, axis=1), "col")
    col_sum = down_columns(jnp.sum(squares, axis=0))
    row_moment = decay_rate * rows_prev + (1.0 - decay_rate) * (row_sum / F + epsilon_one)
    col_moment = decay_rate * cols_prev + (1.0 - decay_rate) * (col_sum / D + epsilon_one)
    factor = row_moment[:, None] * col_moment[None, :]
    raw_update = gradient / jnp.sqrt(factor)
    total_squares = all_total(jnp.sum(raw_update * raw_update))
    clip_scale = jnp.maximum(1.0, jnp.sqrt(total_squares / (D * F)) / clip_level)
    return (raw_update / clip_scale, row_moment, col_moment)


def body(tokens, cotangent, norm_gain, row_prev, col_prev):
    slice_part = lax.psum_scatter(
        gradient_rows(tokens, cotangent, norm_gain), "dp", scatter_dimension=0, tiled=True
    )
    gradient = lax.psum(slice_part, "cuts")
    update, row_moment, col_moment = adafactor_step(
        gradient,
        row_prev[0],
        col_prev,
        lambda values: lax.psum(values, ("dp", "row")),
        lambda values: lax.psum(values, ("dp", "row", "col")),
    )
    return (update[None], row_moment[None], col_moment)


def butterfly(values, axis):
    step = 1
    while step < lax.axis_size(axis):
        pairs = [(i, i ^ step) for i in range(lax.axis_size(axis))]
        values = values + lax.ppermute(values, axis, pairs)
        step *= 2
    return values


def body_swap(tokens, cotangent, norm_gain, row_prev, col_prev):
    n_dp = lax.axis_size("dp")
    d = lax.axis_index("dp")
    rows = tokens.shape[1]
    half = rows // n_dp
    width = half // CHUNKS

    def rows_part(start):
        return lax.dot_general(
            lax.dynamic_slice_in_dim(tokens, start, width, axis=1), cotangent,
            (((0,), (0,)), ((), ())), preferred_element_type=jnp.float32,
        ) * lax.dynamic_slice_in_dim(norm_gain, start, width)[:, None]

    pieces = []
    for c in range(CHUNKS):
        send = rows_part((1 - d) * half + c * width)
        own = rows_part(d * half + c * width)
        slice_sum = own + lax.ppermute(send, "dp", SWAP)
        pieces.append(slice_sum + lax.ppermute(slice_sum, "cuts", SWAP))
    gradient = jnp.concatenate(pieces, axis=0)

    squares = gradient * gradient
    row_sum = butterfly(jnp.sum(squares, axis=1), "col")
    col_sum = butterfly(butterfly(jnp.sum(squares, axis=0), "row"), "dp")

    row_moment = decay_rate * row_prev[0] + (1.0 - decay_rate) * (row_sum / F + epsilon_one)
    col_moment = decay_rate * col_prev + (1.0 - decay_rate) * (col_sum / D + epsilon_one)
    factor = row_moment[:, None] * col_moment[None, :]
    raw_update = gradient / jnp.sqrt(factor)
    total_squares = jnp.sum(raw_update * raw_update)
    for axis in ("row", "dp", "col"):
        total_squares = butterfly(total_squares, axis)
    clip_scale = jnp.maximum(1.0, jnp.sqrt(total_squares / (D * F)) / clip_level)
    return ((raw_update / clip_scale)[None], row_moment[None], col_moment)


def solution(mesh):
    fast = mesh.shape["dp"] == 2 and mesh.shape["cuts"] == 2
    return jax.shard_map(
        body_swap if fast else body,
        mesh=mesh,
        in_specs=(
            P(("cuts", "dp"), "row"),
            P(("cuts", "dp"), "col"),
            P("row"),
            P("row", "dp"),
            P("col"),
        ),
        out_specs=(P("row", "dp", "col"), P("row", "dp"), P("col")),
        check_vma=False,
    )
```

```python
import jax
import jax.numpy as jnp
from jax import lax
from jax.sharding import PartitionSpec as P

D = 4096
F = 4096


decay_rate = 0.975
epsilon_one = 1e-30
clip_level = 1.0

SWAP = [(0, 1), (1, 0)]


def gradient_rows(inputs, cotangent, gains):
    product = lax.dot_general(
        inputs, cotangent, (((0,), (0,)), ((), ())), preferred_element_type=jnp.float32
    )
    return product * gains[:, None]


def adafactor_step(gradient, rows_prev, cols_prev, down_columns, all_total):
    squares = gradient * gradient
    row_sum = lax.psum(jnp.sum(squares, axis=1), "col")
    col_sum = down_columns(jnp.sum(squares, axis=0))
    row_moment = decay_rate * rows_prev + (1.0 - decay_rate) * (row_sum / F + epsilon_one)
    col_moment = decay_rate * cols_prev + (1.0 - decay_rate) * (col_sum / D + epsilon_one)
    factor = row_moment[:, None] * col_moment[None, :]
    raw_update = gradient / jnp.sqrt(factor)
    total_squares = all_total(jnp.sum(raw_update * raw_update))
    clip_scale = jnp.maximum(1.0, jnp.sqrt(total_squares / (D * F)) / clip_level)
    return (raw_update / clip_scale, row_moment, col_moment)


def body(tokens, cotangent, norm_gain, row_prev, col_prev):
    slice_part = lax.psum_scatter(
        gradient_rows(tokens, cotangent, norm_gain), "dp", scatter_dimension=0, tiled=True
    )
    gradient = lax.psum(slice_part, "cuts")
    update, row_moment, col_moment = adafactor_step(
        gradient,
        row_prev[0],
        col_prev,
        lambda values: lax.psum(values, ("dp", "row")),
        lambda values: lax.psum(values, ("dp", "row", "col")),
    )
    return (update[None], row_moment[None], col_moment)


def butterfly(values, axis):
    step = 1
    while step < lax.axis_size(axis):
        pairs = [(i, i ^ step) for i in range(lax.axis_size(axis))]
        values = values + lax.ppermute(values, axis, pairs)
        step *= 2
    return values


def body_swap(tokens, cotangent, norm_gain, row_prev, col_prev):
    n_dp = lax.axis_size("dp")
    d = lax.axis_index("dp")
    rows = tokens.shape[1]
    half = rows // n_dp
    widths = [half // 8] * 7 + [half // 16] * 2

    def rows_part(start, width):
        return lax.dot_general(
            lax.dynamic_slice_in_dim(tokens, start, width, axis=1), cotangent,
            (((0,), (0,)), ((), ())), preferred_element_type=jnp.float32,
        ) * lax.dynamic_slice_in_dim(norm_gain, start, width)[:, None]

    pieces = []
    offset = 0
    for width in widths:
        send = rows_part((1 - d) * half + offset, width)
        own = rows_part(d * half + offset, width)
        slice_sum = own + lax.ppermute(send, "dp", SWAP)
        pieces.append(slice_sum + lax.ppermute(slice_sum, "cuts", SWAP))
        offset += width

    row_sum = jnp.concatenate([jnp.sum(p * p, axis=1) for p in pieces])
    col_sum = sum(jnp.sum(p * p, axis=0) for p in pieces)
    col_sum = butterfly(butterfly(col_sum, "row"), "dp")
    col_moment = decay_rate * col_prev + (1.0 - decay_rate) * (col_sum / D + epsilon_one)
    weighted = jnp.concatenate([jnp.sum(p * p / col_moment[None, :], axis=1) for p in pieces])
    both = butterfly(jnp.stack([row_sum, weighted]), "col")
    row_moment = decay_rate * row_prev[0] + (1.0 - decay_rate) * (both[0] / F + epsilon_one)
    total_squares = jnp.sum(both[1] / row_moment)
    for axis in ("row", "dp"):
        total_squares = butterfly(total_squares, axis)
    clip_scale = jnp.maximum(1.0, jnp.sqrt(total_squares / (D * F)) / clip_level)
    gradient = jnp.concatenate(pieces, axis=0)
    factor = row_moment[:, None] * col_moment[None, :]
    raw_update = gradient / jnp.sqrt(factor)
    return ((raw_update / clip_scale)[None], row_moment[None], col_moment)


def solution(mesh):
    fast = mesh.shape["dp"] == 2 and mesh.shape["cuts"] == 2
    return jax.shard_map(
        body_swap if fast else body,
        mesh=mesh,
        in_specs=(
            P(("cuts", "dp"), "row"),
            P(("cuts", "dp"), "col"),
            P("row"),
            P("row", "dp"),
            P("col"),
        ),
        out_specs=(P("row", "dp", "col"), P("row", "dp"), P("col")),
        check_vma=False,
    )
```

```python
import jax
import jax.numpy as jnp
from jax import lax
from jax.sharding import PartitionSpec as P

D = 4096
F = 4096


decay_rate = 0.975
epsilon_one = 1e-30
clip_level = 1.0

SWAP = [(0, 1), (1, 0)]


def gradient_rows(inputs, cotangent, gains):
    product = lax.dot_general(
        inputs, cotangent, (((0,), (0,)), ((), ())), preferred_element_type=jnp.float32
    )
    return product * gains[:, None]


def adafactor_step(gradient, rows_prev, cols_prev, down_columns, all_total):
    squares = gradient * gradient
    row_sum = lax.psum(jnp.sum(squares, axis=1), "col")
    col_sum = down_columns(jnp.sum(squares, axis=0))
    row_moment = decay_rate * rows_prev + (1.0 - decay_rate) * (row_sum / F + epsilon_one)
    col_moment = decay_rate * cols_prev + (1.0 - decay_rate) * (col_sum / D + epsilon_one)
    factor = row_moment[:, None] * col_moment[None, :]
    raw_update = gradient / jnp.sqrt(factor)
    total_squares = all_total(jnp.sum(raw_update * raw_update))
    clip_scale = jnp.maximum(1.0, jnp.sqrt(total_squares / (D * F)) / clip_level)
    return (raw_update / clip_scale, row_moment, col_moment)


def body(tokens, cotangent, norm_gain, row_prev, col_prev):
    slice_part = lax.psum_scatter(
        gradient_rows(tokens, cotangent, norm_gain), "dp", scatter_dimension=0, tiled=True
    )
    gradient = lax.psum(slice_part, "cuts")
    update, row_moment, col_moment = adafactor_step(
        gradient,
        row_prev[0],
        col_prev,
        lambda values: lax.psum(values, ("dp", "row")),
        lambda values: lax.psum(values, ("dp", "row", "col")),
    )
    return (update[None], row_moment[None], col_moment)


def butterfly(values, axis):
    step = 1
    while step < lax.axis_size(axis):
        pairs = [(i, i ^ step) for i in range(lax.axis_size(axis))]
        values = values + lax.ppermute(values, axis, pairs)
        step *= 2
    return values


def body_swap(tokens, cotangent, norm_gain, row_prev, col_prev):
    n_dp = lax.axis_size("dp")
    d = lax.axis_index("dp")
    rows = tokens.shape[1]
    half = rows // n_dp
    widths = [half // 8] * 8

    def rows_part(start, width):
        return lax.dot_general(
            lax.dynamic_slice_in_dim(tokens, start, width, axis=1), cotangent,
            (((0,), (0,)), ((), ())), preferred_element_type=jnp.float32,
        ) * lax.dynamic_slice_in_dim(norm_gain, start, width)[:, None]

    pieces = []
    offset = 0
    for width in widths:
        send = rows_part((1 - d) * half + offset, width)
        own = rows_part(d * half + offset, width)
        slice_sum = own + lax.ppermute(send, "dp", SWAP)
        pieces.append(slice_sum + lax.ppermute(slice_sum, "cuts", SWAP))
        offset += width

    row_sum = jnp.concatenate([jnp.sum(p * p, axis=1) for p in pieces])
    col_sum = sum(jnp.sum(p * p, axis=0) for p in pieces)
    col_sum = butterfly(butterfly(col_sum, "row"), "dp")
    col_moment = decay_rate * col_prev + (1.0 - decay_rate) * (col_sum / D + epsilon_one)
    col_inverse = 1.0 / col_moment
    weighted = jnp.concatenate([jnp.sum(p * p * col_inverse[None, :], axis=1) for p in pieces])
    both = butterfly(jnp.stack([row_sum, weighted]), "col")
    row_moment = decay_rate * row_prev[0] + (1.0 - decay_rate) * (both[0] / F + epsilon_one)
    total_squares = jnp.sum(both[1] / row_moment)
    for axis in ("row", "dp"):
        total_squares = butterfly(total_squares, axis)
    clip_scale = jnp.maximum(1.0, jnp.sqrt(total_squares / (D * F)) / clip_level)
    row_scale = 1.0 / (jnp.sqrt(row_moment) * clip_scale)
    col_scale = 1.0 / jnp.sqrt(col_moment)
    update = []
    offset = 0
    for p in pieces:
        update.append(p * row_scale[offset:offset + p.shape[0], None] * col_scale[None, :])
        offset += p.shape[0]
    return (jnp.concatenate(update, axis=0)[None], row_moment[None], col_moment)


def solution(mesh):
    fast = mesh.shape["dp"] == 2 and mesh.shape["cuts"] == 2
    return jax.shard_map(
        body_swap if fast else body,
        mesh=mesh,
        in_specs=(
            P(("cuts", "dp"), "row"),
            P(("cuts", "dp"), "col"),
            P("row"),
            P("row", "dp"),
            P("col"),
        ),
        out_specs=(P("row", "dp", "col"), P("row", "dp"), P("col")),
        check_vma=False,
    )
```

```python
import jax
import jax.numpy as jnp
from jax import lax
from jax.sharding import PartitionSpec as P

D = 4096
F = 4096


decay_rate = 0.975
epsilon_one = 1e-30
clip_level = 1.0

SWAP = [(0, 1), (1, 0)]


def gradient_rows(inputs, cotangent, gains):
    product = lax.dot_general(
        inputs, cotangent, (((0,), (0,)), ((), ())), preferred_element_type=jnp.float32
    )
    return product * gains[:, None]


def adafactor_step(gradient, rows_prev, cols_prev, down_columns, all_total):
    squares = gradient * gradient
    row_sum = lax.psum(jnp.sum(squares, axis=1), "col")
    col_sum = down_columns(jnp.sum(squares, axis=0))
    row_moment = decay_rate * rows_prev + (1.0 - decay_rate) * (row_sum / F + epsilon_one)
    col_moment = decay_rate * cols_prev + (1.0 - decay_rate) * (col_sum / D + epsilon_one)
    factor = row_moment[:, None] * col_moment[None, :]
    raw_update = gradient / jnp.sqrt(factor)
    total_squares = all_total(jnp.sum(raw_update * raw_update))
    clip_scale = jnp.maximum(1.0, jnp.sqrt(total_squares / (D * F)) / clip_level)
    return (raw_update / clip_scale, row_moment, col_moment)


def body(tokens, cotangent, norm_gain, row_prev, col_prev):
    slice_part = lax.psum_scatter(
        gradient_rows(tokens, cotangent, norm_gain), "dp", scatter_dimension=0, tiled=True
    )
    gradient = lax.psum(slice_part, "cuts")
    update, row_moment, col_moment = adafactor_step(
        gradient,
        row_prev[0],
        col_prev,
        lambda values: lax.psum(values, ("dp", "row")),
        lambda values: lax.psum(values, ("dp", "row", "col")),
    )
    return (update[None], row_moment[None], col_moment)


def butterfly(values, axis):
    step = 1
    while step < lax.axis_size(axis):
        pairs = [(i, i ^ step) for i in range(lax.axis_size(axis))]
        values = values + lax.ppermute(values, axis, pairs)
        step *= 2
    return values


def body_swap(tokens, cotangent, norm_gain, row_prev, col_prev):
    n_dp = lax.axis_size("dp")
    d = lax.axis_index("dp")
    rows = tokens.shape[1]
    half = rows // n_dp
    unit = half // 32
    widths = [unit, 3 * unit] + [4 * unit] * 6 + [2 * unit] * 2

    def rows_part(start, width):
        return lax.dot_general(
            lax.dynamic_slice_in_dim(tokens, start, width, axis=1), cotangent,
            (((0,), (0,)), ((), ())), preferred_element_type=jnp.float32,
        ) * lax.dynamic_slice_in_dim(norm_gain, start, width)[:, None]

    pieces = []
    offset = 0
    for width in widths:
        send = rows_part((1 - d) * half + offset, width)
        own = rows_part(d * half + offset, width)
        slice_sum = own + lax.ppermute(send, "dp", SWAP)
        pieces.append(slice_sum + lax.ppermute(slice_sum, "cuts", SWAP))
        offset += width

    row_sum = jnp.concatenate([jnp.sum(p * p, axis=1) for p in pieces])
    col_sum = sum(jnp.sum(p * p, axis=0) for p in pieces)
    col_sum = butterfly(butterfly(col_sum, "row"), "dp")
    col_moment = decay_rate * col_prev + (1.0 - decay_rate) * (col_sum / D + epsilon_one)
    col_inverse = 1.0 / col_moment
    weighted = jnp.concatenate([jnp.sum(p * p * col_inverse[None, :], axis=1) for p in pieces])
    both = butterfly(jnp.stack([row_sum, weighted]), "col")
    row_moment = decay_rate * row_prev[0] + (1.0 - decay_rate) * (both[0] / F + epsilon_one)
    total_squares = jnp.sum(both[1] / row_moment)
    for axis in ("row", "dp"):
        total_squares = butterfly(total_squares, axis)
    clip_scale = jnp.maximum(1.0, jnp.sqrt(total_squares / (D * F)) / clip_level)
    row_scale = 1.0 / (jnp.sqrt(row_moment) * clip_scale)
    col_scale = 1.0 / jnp.sqrt(col_moment)
    update = []
    offset = 0
    for p in pieces:
        update.append(p * row_scale[offset:offset + p.shape[0], None] * col_scale[None, :])
        offset += p.shape[0]
    return (jnp.concatenate(update, axis=0)[None], row_moment[None], col_moment)


def solution(mesh):
    fast = mesh.shape["dp"] == 2 and mesh.shape["cuts"] == 2
    return jax.shard_map(
        body_swap if fast else body,
        mesh=mesh,
        in_specs=(
            P(("cuts", "dp"), "row"),
            P(("cuts", "dp"), "col"),
            P("row"),
            P("row", "dp"),
            P("col"),
        ),
        out_specs=(P("row", "dp", "col"), P("row", "dp"), P("col")),
        check_vma=False,
    )
```

```python
import jax
import jax.numpy as jnp
from jax import lax
from jax.sharding import PartitionSpec as P

D = 4096
F = 4096


decay_rate = 0.975
epsilon_one = 1e-30
clip_level = 1.0

SWAP = [(0, 1), (1, 0)]
LAG = 3


def gradient_rows(inputs, cotangent, gains):
    product = lax.dot_general(
        inputs, cotangent, (((0,), (0,)), ((), ())), preferred_element_type=jnp.float32
    )
    return product * gains[:, None]


def adafactor_step(gradient, rows_prev, cols_prev, down_columns, all_total):
    squares = gradient * gradient
    row_sum = lax.psum(jnp.sum(squares, axis=1), "col")
    col_sum = down_columns(jnp.sum(squares, axis=0))
    row_moment = decay_rate * rows_prev + (1.0 - decay_rate) * (row_sum / F + epsilon_one)
    col_moment = decay_rate * cols_prev + (1.0 - decay_rate) * (col_sum / D + epsilon_one)
    factor = row_moment[:, None] * col_moment[None, :]
    raw_update = gradient / jnp.sqrt(factor)
    total_squares = all_total(jnp.sum(raw_update * raw_update))
    clip_scale = jnp.maximum(1.0, jnp.sqrt(total_squares / (D * F)) / clip_level)
    return (raw_update / clip_scale, row_moment, col_moment)


def body(tokens, cotangent, norm_gain, row_prev, col_prev):
    slice_part = lax.psum_scatter(
        gradient_rows(tokens, cotangent, norm_gain), "dp", scatter_dimension=0, tiled=True
    )
    gradient = lax.psum(slice_part, "cuts")
    update, row_moment, col_moment = adafactor_step(
        gradient,
        row_prev[0],
        col_prev,
        lambda values: lax.psum(values, ("dp", "row")),
        lambda values: lax.psum(values, ("dp", "row", "col")),
    )
    return (update[None], row_moment[None], col_moment)


def butterfly(values, axis):
    step = 1
    while step < lax.axis_size(axis):
        pairs = [(i, i ^ step) for i in range(lax.axis_size(axis))]
        values = values + lax.ppermute(values, axis, pairs)
        step *= 2
    return values


def body_swap(tokens, cotangent, norm_gain, row_prev, col_prev):
    n_dp = lax.axis_size("dp")
    d = lax.axis_index("dp")
    rows = tokens.shape[1]
    half = rows // n_dp
    unit = half // 32
    widths = [unit, 3 * unit] + [4 * unit] * 6 + [2 * unit] * 2

    def rows_part(start, width):
        return lax.dot_general(
            lax.dynamic_slice_in_dim(tokens, start, width, axis=1), cotangent,
            (((0,), (0,)), ((), ())), preferred_element_type=jnp.float32,
        ) * lax.dynamic_slice_in_dim(norm_gain, start, width)[:, None]

    pieces = []
    sums = []
    offset = 0
    for width in widths:
        send = rows_part((1 - d) * half + offset, width)
        if len(sums) >= LAG:
            send, _ = lax.optimization_barrier((send, sums[-LAG]))
        own = rows_part(d * half + offset, width)
        sums.append(own + lax.ppermute(send, "dp", SWAP))
        pieces.append(sums[-1] + lax.ppermute(sums[-1], "cuts", SWAP))
        offset += width

    row_sum = jnp.concatenate([jnp.sum(p * p, axis=1) for p in pieces])
    col_sum = sum(jnp.sum(p * p, axis=0) for p in pieces)
    col_sum = butterfly(butterfly(col_sum, "row"), "dp")
    col_moment = decay_rate * col_prev + (1.0 - decay_rate) * (col_sum / D + epsilon_one)
    col_inverse = 1.0 / col_moment
    weighted = jnp.concatenate([jnp.sum(p * p * col_inverse[None, :], axis=1) for p in pieces])
    both = butterfly(jnp.stack([row_sum, weighted]), "col")
    row_moment = decay_rate * row_prev[0] + (1.0 - decay_rate) * (both[0] / F + epsilon_one)
    total_squares = jnp.sum(both[1] / row_moment)
    for axis in ("row", "dp"):
        total_squares = butterfly(total_squares, axis)
    clip_scale = jnp.maximum(1.0, jnp.sqrt(total_squares / (D * F)) / clip_level)
    row_scale = 1.0 / (jnp.sqrt(row_moment) * clip_scale)
    col_scale = 1.0 / jnp.sqrt(col_moment)
    update = []
    offset = 0
    for p in pieces:
        update.append(p * row_scale[offset:offset + p.shape[0], None] * col_scale[None, :])
        offset += p.shape[0]
    return (jnp.concatenate(update, axis=0)[None], row_moment[None], col_moment)


def solution(mesh):
    fast = mesh.shape["dp"] == 2 and mesh.shape["cuts"] == 2
    return jax.shard_map(
        body_swap if fast else body,
        mesh=mesh,
        in_specs=(
            P(("cuts", "dp"), "row"),
            P(("cuts", "dp"), "col"),
            P("row"),
            P("row", "dp"),
            P("col"),
        ),
        out_specs=(P("row", "dp", "col"), P("row", "dp"), P("col")),
        check_vma=False,
    )
```

```python
import jax
import jax.numpy as jnp
from jax import lax
from jax.sharding import PartitionSpec as P

D = 4096
F = 4096


decay_rate = 0.975
epsilon_one = 1e-30
clip_level = 1.0

SWAP = [(0, 1), (1, 0)]
CHUNKS = 8
LAG = 3


def gradient_rows(inputs, cotangent, gains):
    product = lax.dot_general(
        inputs, cotangent, (((0,), (0,)), ((), ())), preferred_element_type=jnp.float32
    )
    return product * gains[:, None]


def adafactor_step(gradient, rows_prev, cols_prev, down_columns, all_total):
    squares = gradient * gradient
    row_sum = lax.psum(jnp.sum(squares, axis=1), "col")
    col_sum = down_columns(jnp.sum(squares, axis=0))
    row_moment = decay_rate * rows_prev + (1.0 - decay_rate) * (row_sum / F + epsilon_one)
    col_moment = decay_rate * cols_prev + (1.0 - decay_rate) * (col_sum / D + epsilon_one)
    factor = row_moment[:, None] * col_moment[None, :]
    raw_update = gradient / jnp.sqrt(factor)
    total_squares = all_total(jnp.sum(raw_update * raw_update))
    clip_scale = jnp.maximum(1.0, jnp.sqrt(total_squares / (D * F)) / clip_level)
    return (raw_update / clip_scale, row_moment, col_moment)


def body(tokens, cotangent, norm_gain, row_prev, col_prev):
    slice_part = lax.psum_scatter(
        gradient_rows(tokens, cotangent, norm_gain), "dp", scatter_dimension=0, tiled=True
    )
    gradient = lax.psum(slice_part, "cuts")
    update, row_moment, col_moment = adafactor_step(
        gradient,
        row_prev[0],
        col_prev,
        lambda values: lax.psum(values, ("dp", "row")),
        lambda values: lax.psum(values, ("dp", "row", "col")),
    )
    return (update[None], row_moment[None], col_moment)


def butterfly(values, axis):
    step = 1
    while step < lax.axis_size(axis):
        pairs = [(i, i ^ step) for i in range(lax.axis_size(axis))]
        values = values + lax.ppermute(values, axis, pairs)
        step *= 2
    return values


def body_swap(tokens, cotangent, norm_gain, row_prev, col_prev):
    n_dp = lax.axis_size("dp")
    d = lax.axis_index("dp")
    rows = tokens.shape[1]
    half = rows // n_dp
    width = half // CHUNKS

    def rows_part(start):
        return lax.dot_general(
            lax.dynamic_slice_in_dim(tokens, start, width, axis=1), cotangent,
            (((0,), (0,)), ((), ())), preferred_element_type=jnp.float32,
        ) * lax.dynamic_slice_in_dim(norm_gain, start, width)[:, None]

    pieces = []
    sums = []
    for c in range(CHUNKS):
        send = rows_part((1 - d) * half + c * width)
        if len(sums) >= LAG:
            send, _ = lax.optimization_barrier((send, sums[-LAG]))
        own = rows_part(d * half + c * width)
        sums.append(own + lax.ppermute(send, "dp", SWAP))
        pieces.append(sums[-1] + lax.ppermute(sums[-1], "cuts", SWAP))
    gradient = jnp.concatenate(pieces, axis=0)

    squares = gradient * gradient
    row_sum = butterfly(jnp.sum(squares, axis=1), "col")
    col_sum = butterfly(butterfly(jnp.sum(squares, axis=0), "row"), "dp")

    row_moment = decay_rate * row_prev[0] + (1.0 - decay_rate) * (row_sum / F + epsilon_one)
    col_moment = decay_rate * col_prev + (1.0 - decay_rate) * (col_sum / D + epsilon_one)
    factor = row_moment[:, None] * col_moment[None, :]
    raw_update = gradient / jnp.sqrt(factor)
    total_squares = jnp.sum(raw_update * raw_update)
    for axis in ("row", "dp", "col"):
        total_squares = butterfly(total_squares, axis)
    clip_scale = jnp.maximum(1.0, jnp.sqrt(total_squares / (D * F)) / clip_level)
    return ((raw_update / clip_scale)[None], row_moment[None], col_moment)


def solution(mesh):
    fast = mesh.shape["dp"] == 2 and mesh.shape["cuts"] == 2
    return jax.shard_map(
        body_swap if fast else body,
        mesh=mesh,
        in_specs=(
            P(("cuts", "dp"), "row"),
            P(("cuts", "dp"), "col"),
            P("row"),
            P("row", "dp"),
            P("col"),
        ),
        out_specs=(P("row", "dp", "col"), P("row", "dp"), P("col")),
        check_vma=False,
    )
```

```python
import jax
import jax.numpy as jnp
from jax import lax
from jax.sharding import PartitionSpec as P

D = 4096
F = 4096


decay_rate = 0.975
epsilon_one = 1e-30
clip_level = 1.0

SWAP = [(0, 1), (1, 0)]
LAG = 3


def gradient_rows(inputs, cotangent, gains):
    product = lax.dot_general(
        inputs, cotangent, (((0,), (0,)), ((), ())), preferred_element_type=jnp.float32
    )
    return product * gains[:, None]


def adafactor_step(gradient, rows_prev, cols_prev, down_columns, all_total):
    squares = gradient * gradient
    row_sum = lax.psum(jnp.sum(squares, axis=1), "col")
    col_sum = down_columns(jnp.sum(squares, axis=0))
    row_moment = decay_rate * rows_prev + (1.0 - decay_rate) * (row_sum / F + epsilon_one)
    col_moment = decay_rate * cols_prev + (1.0 - decay_rate) * (col_sum / D + epsilon_one)
    factor = row_moment[:, None] * col_moment[None, :]
    raw_update = gradient / jnp.sqrt(factor)
    total_squares = all_total(jnp.sum(raw_update * raw_update))
    clip_scale = jnp.maximum(1.0, jnp.sqrt(total_squares / (D * F)) / clip_level)
    return (raw_update / clip_scale, row_moment, col_moment)


def body(tokens, cotangent, norm_gain, row_prev, col_prev):
    slice_part = lax.psum_scatter(
        gradient_rows(tokens, cotangent, norm_gain), "dp", scatter_dimension=0, tiled=True
    )
    gradient = lax.psum(slice_part, "cuts")
    update, row_moment, col_moment = adafactor_step(
        gradient,
        row_prev[0],
        col_prev,
        lambda values: lax.psum(values, ("dp", "row")),
        lambda values: lax.psum(values, ("dp", "row", "col")),
    )
    return (update[None], row_moment[None], col_moment)


def butterfly(values, axis):
    step = 1
    while step < lax.axis_size(axis):
        pairs = [(i, i ^ step) for i in range(lax.axis_size(axis))]
        values = values + lax.ppermute(values, axis, pairs)
        step *= 2
    return values


def body_swap(tokens, cotangent, norm_gain, row_prev, col_prev):
    n_dp = lax.axis_size("dp")
    d = lax.axis_index("dp")
    rows = tokens.shape[1]
    half = rows // n_dp
    unit = half // 32
    widths = [unit, 3 * unit] + [4 * unit] * 6 + [2 * unit] * 2

    def rows_part(start, width):
        return lax.dot_general(
            lax.dynamic_slice_in_dim(tokens, start, width, axis=1), cotangent,
            (((0,), (0,)), ((), ())), preferred_element_type=jnp.float32,
        ) * lax.dynamic_slice_in_dim(norm_gain, start, width)[:, None]

    pieces = []
    sums = []
    offset = 0
    for width in widths:
        send = rows_part((1 - d) * half + offset, width)
        if len(sums) >= LAG:
            send, _ = lax.optimization_barrier((send, sums[-LAG]))
        own = rows_part(d * half + offset, width)
        sums.append(own + lax.ppermute(send, "dp", SWAP))
        pieces.append(sums[-1] + lax.ppermute(sums[-1], "cuts", SWAP))
        offset += width
    gradient = jnp.concatenate(pieces, axis=0)

    squares = gradient * gradient
    col_sum = butterfly(butterfly(jnp.sum(squares, axis=0), "row"), "dp")
    col_moment = decay_rate * col_prev + (1.0 - decay_rate) * (col_sum / D + epsilon_one)
    weighted = jnp.sum(squares * (1.0 / col_moment)[None, :], axis=1)
    both = butterfly(jnp.stack([jnp.sum(squares, axis=1), weighted]), "col")
    row_moment = decay_rate * row_prev[0] + (1.0 - decay_rate) * (both[0] / F + epsilon_one)
    total_squares = jnp.sum(both[1] / row_moment)
    for axis in ("row", "dp"):
        total_squares = butterfly(total_squares, axis)
    clip_scale = jnp.maximum(1.0, jnp.sqrt(total_squares / (D * F)) / clip_level)
    factor = row_moment[:, None] * col_moment[None, :]
    raw_update = gradient / jnp.sqrt(factor)
    return ((raw_update / clip_scale)[None], row_moment[None], col_moment)


def solution(mesh):
    fast = mesh.shape["dp"] == 2 and mesh.shape["cuts"] == 2
    return jax.shard_map(
        body_swap if fast else body,
        mesh=mesh,
        in_specs=(
            P(("cuts", "dp"), "row"),
            P(("cuts", "dp"), "col"),
            P("row"),
            P("row", "dp"),
            P("col"),
        ),
        out_specs=(P("row", "dp", "col"), P("row", "dp"), P("col")),
        check_vma=False,
    )
```

```python
import jax
import jax.numpy as jnp
from jax import lax
from jax.sharding import PartitionSpec as P

D = 4096
F = 4096


decay_rate = 0.975
epsilon_one = 1e-30
clip_level = 1.0

SWAP = [(0, 1), (1, 0)]
LAG = 3


def gradient_rows(inputs, cotangent, gains):
    product = lax.dot_general(
        inputs, cotangent, (((0,), (0,)), ((), ())), preferred_element_type=jnp.float32
    )
    return product * gains[:, None]


def adafactor_step(gradient, rows_prev, cols_prev, down_columns, all_total):
    squares = gradient * gradient
    row_sum = lax.psum(jnp.sum(squares, axis=1), "col")
    col_sum = down_columns(jnp.sum(squares, axis=0))
    row_moment = decay_rate * rows_prev + (1.0 - decay_rate) * (row_sum / F + epsilon_one)
    col_moment = decay_rate * cols_prev + (1.0 - decay_rate) * (col_sum / D + epsilon_one)
    factor = row_moment[:, None] * col_moment[None, :]
    raw_update = gradient / jnp.sqrt(factor)
    total_squares = all_total(jnp.sum(raw_update * raw_update))
    clip_scale = jnp.maximum(1.0, jnp.sqrt(total_squares / (D * F)) / clip_level)
    return (raw_update / clip_scale, row_moment, col_moment)


def body(tokens, cotangent, norm_gain, row_prev, col_prev):
    slice_part = lax.psum_scatter(
        gradient_rows(tokens, cotangent, norm_gain), "dp", scatter_dimension=0, tiled=True
    )
    gradient = lax.psum(slice_part, "cuts")
    update, row_moment, col_moment = adafactor_step(
        gradient,
        row_prev[0],
        col_prev,
        lambda values: lax.psum(values, ("dp", "row")),
        lambda values: lax.psum(values, ("dp", "row", "col")),
    )
    return (update[None], row_moment[None], col_moment)


def butterfly(values, axis):
    step = 1
    while step < lax.axis_size(axis):
        pairs = [(i, i ^ step) for i in range(lax.axis_size(axis))]
        values = values + lax.ppermute(values, axis, pairs)
        step *= 2
    return values


def body_swap(tokens, cotangent, norm_gain, row_prev, col_prev):
    n_dp = lax.axis_size("dp")
    d = lax.axis_index("dp")
    rows = tokens.shape[1]
    half = rows // n_dp
    widths = [half // 8] * 8

    def rows_part(start, width):
        return lax.dot_general(
            lax.dynamic_slice_in_dim(tokens, start, width, axis=1), cotangent,
            (((0,), (0,)), ((), ())), preferred_element_type=jnp.float32,
        ) * lax.dynamic_slice_in_dim(norm_gain, start, width)[:, None]

    pieces = []
    sums = []
    offset = 0
    for width in widths:
        send = rows_part((1 - d) * half + offset, width)
        if len(sums) >= LAG:
            send, _ = lax.optimization_barrier((send, sums[-LAG]))
        own = rows_part(d * half + offset, width)
        sums.append(own + lax.ppermute(send, "dp", SWAP))
        pieces.append(sums[-1] + lax.ppermute(sums[-1], "cuts", SWAP))
        offset += width
    gradient = jnp.concatenate(pieces, axis=0)

    squares = gradient * gradient
    col_sum = butterfly(butterfly(jnp.sum(squares, axis=0), "row"), "dp")
    col_moment = decay_rate * col_prev + (1.0 - decay_rate) * (col_sum / D + epsilon_one)
    weighted = jnp.sum(squares * (1.0 / col_moment)[None, :], axis=1)
    both = butterfly(jnp.stack([jnp.sum(squares, axis=1), weighted]), "col")
    row_moment = decay_rate * row_prev[0] + (1.0 - decay_rate) * (both[0] / F + epsilon_one)
    total_squares = jnp.sum(both[1] / row_moment)
    for axis in ("row", "dp"):
        total_squares = butterfly(total_squares, axis)
    clip_scale = jnp.maximum(1.0, jnp.sqrt(total_squares / (D * F)) / clip_level)
    factor = row_moment[:, None] * col_moment[None, :]
    raw_update = gradient / jnp.sqrt(factor)
    return ((raw_update / clip_scale)[None], row_moment[None], col_moment)


def solution(mesh):
    fast = mesh.shape["dp"] == 2 and mesh.shape["cuts"] == 2
    return jax.shard_map(
        body_swap if fast else body,
        mesh=mesh,
        in_specs=(
            P(("cuts", "dp"), "row"),
            P(("cuts", "dp"), "col"),
            P("row"),
            P("row", "dp"),
            P("col"),
        ),
        out_specs=(P("row", "dp", "col"), P("row", "dp"), P("col")),
        check_vma=False,
    )
```

```python
import jax
import jax.numpy as jnp
from jax import lax
from jax.sharding import PartitionSpec as P

D = 4096
F = 4096


decay_rate = 0.975
epsilon_one = 1e-30
clip_level = 1.0

SWAP = [(0, 1), (1, 0)]
LAG = 4


def gradient_rows(inputs, cotangent, gains):
    product = lax.dot_general(
        inputs, cotangent, (((0,), (0,)), ((), ())), preferred_element_type=jnp.float32
    )
    return product * gains[:, None]


def adafactor_step(gradient, rows_prev, cols_prev, down_columns, all_total):
    squares = gradient * gradient
    row_sum = lax.psum(jnp.sum(squares, axis=1), "col")
    col_sum = down_columns(jnp.sum(squares, axis=0))
    row_moment = decay_rate * rows_prev + (1.0 - decay_rate) * (row_sum / F + epsilon_one)
    col_moment = decay_rate * cols_prev + (1.0 - decay_rate) * (col_sum / D + epsilon_one)
    factor = row_moment[:, None] * col_moment[None, :]
    raw_update = gradient / jnp.sqrt(factor)
    total_squares = all_total(jnp.sum(raw_update * raw_update))
    clip_scale = jnp.maximum(1.0, jnp.sqrt(total_squares / (D * F)) / clip_level)
    return (raw_update / clip_scale, row_moment, col_moment)


def body(tokens, cotangent, norm_gain, row_prev, col_prev):
    slice_part = lax.psum_scatter(
        gradient_rows(tokens, cotangent, norm_gain), "dp", scatter_dimension=0, tiled=True
    )
    gradient = lax.psum(slice_part, "cuts")
    update, row_moment, col_moment = adafactor_step(
        gradient,
        row_prev[0],
        col_prev,
        lambda values: lax.psum(values, ("dp", "row")),
        lambda values: lax.psum(values, ("dp", "row", "col")),
    )
    return (update[None], row_moment[None], col_moment)


def butterfly(values, axis):
    step = 1
    while step < lax.axis_size(axis):
        pairs = [(i, i ^ step) for i in range(lax.axis_size(axis))]
        values = values + lax.ppermute(values, axis, pairs)
        step *= 2
    return values


def body_swap(tokens, cotangent, norm_gain, row_prev, col_prev):
    n_dp = lax.axis_size("dp")
    d = lax.axis_index("dp")
    rows = tokens.shape[1]
    half = rows // n_dp
    widths = [half // 16] * 16

    def rows_part(start, width):
        return lax.dot_general(
            lax.dynamic_slice_in_dim(tokens, start, width, axis=1), cotangent,
            (((0,), (0,)), ((), ())), preferred_element_type=jnp.float32,
        ) * lax.dynamic_slice_in_dim(norm_gain, start, width)[:, None]

    pieces = []
    sums = []
    offset = 0
    for width in widths:
        send = rows_part((1 - d) * half + offset, width)
        if len(sums) >= LAG:
            send, _ = lax.optimization_barrier((send, sums[-LAG]))
        own = rows_part(d * half + offset, width)
        sums.append(own + lax.ppermute(send, "dp", SWAP))
        pieces.append(sums[-1] + lax.ppermute(sums[-1], "cuts", SWAP))
        offset += width
    gradient = jnp.concatenate(pieces, axis=0)

    squares = gradient * gradient
    col_sum = butterfly(butterfly(jnp.sum(squares, axis=0), "row"), "dp")
    col_moment = decay_rate * col_prev + (1.0 - decay_rate) * (col_sum / D + epsilon_one)
    weighted = jnp.sum(squares * (1.0 / col_moment)[None, :], axis=1)
    both = butterfly(jnp.stack([jnp.sum(squares, axis=1), weighted]), "col")
    row_moment = decay_rate * row_prev[0] + (1.0 - decay_rate) * (both[0] / F + epsilon_one)
    total_squares = jnp.sum(both[1] / row_moment)
    for axis in ("row", "dp"):
        total_squares = butterfly(total_squares, axis)
    clip_scale = jnp.maximum(1.0, jnp.sqrt(total_squares / (D * F)) / clip_level)
    factor = row_moment[:, None] * col_moment[None, :]
    raw_update = gradient / jnp.sqrt(factor)
    return ((raw_update / clip_scale)[None], row_moment[None], col_moment)


def solution(mesh):
    fast = mesh.shape["dp"] == 2 and mesh.shape["cuts"] == 2
    return jax.shard_map(
        body_swap if fast else body,
        mesh=mesh,
        in_specs=(
            P(("cuts", "dp"), "row"),
            P(("cuts", "dp"), "col"),
            P("row"),
            P("row", "dp"),
            P("col"),
        ),
        out_specs=(P("row", "dp", "col"), P("row", "dp"), P("col")),
        check_vma=False,
    )
```

```python
import jax
import jax.numpy as jnp
from jax import lax
from jax.sharding import PartitionSpec as P

D = 4096
F = 4096


decay_rate = 0.975
epsilon_one = 1e-30
clip_level = 1.0

SWAP = [(0, 1), (1, 0)]
LAG = 2


def gradient_rows(inputs, cotangent, gains):
    product = lax.dot_general(
        inputs, cotangent, (((0,), (0,)), ((), ())), preferred_element_type=jnp.float32
    )
    return product * gains[:, None]


def adafactor_step(gradient, rows_prev, cols_prev, down_columns, all_total):
    squares = gradient * gradient
    row_sum = lax.psum(jnp.sum(squares, axis=1), "col")
    col_sum = down_columns(jnp.sum(squares, axis=0))
    row_moment = decay_rate * rows_prev + (1.0 - decay_rate) * (row_sum / F + epsilon_one)
    col_moment = decay_rate * cols_prev + (1.0 - decay_rate) * (col_sum / D + epsilon_one)
    factor = row_moment[:, None] * col_moment[None, :]
    raw_update = gradient / jnp.sqrt(factor)
    total_squares = all_total(jnp.sum(raw_update * raw_update))
    clip_scale = jnp.maximum(1.0, jnp.sqrt(total_squares / (D * F)) / clip_level)
    return (raw_update / clip_scale, row_moment, col_moment)


def body(tokens, cotangent, norm_gain, row_prev, col_prev):
    slice_part = lax.psum_scatter(
        gradient_rows(tokens, cotangent, norm_gain), "dp", scatter_dimension=0, tiled=True
    )
    gradient = lax.psum(slice_part, "cuts")
    update, row_moment, col_moment = adafactor_step(
        gradient,
        row_prev[0],
        col_prev,
        lambda values: lax.psum(values, ("dp", "row")),
        lambda values: lax.psum(values, ("dp", "row", "col")),
    )
    return (update[None], row_moment[None], col_moment)


def butterfly(values, axis):
    step = 1
    while step < lax.axis_size(axis):
        pairs = [(i, i ^ step) for i in range(lax.axis_size(axis))]
        values = values + lax.ppermute(values, axis, pairs)
        step *= 2
    return values


def body_swap(tokens, cotangent, norm_gain, row_prev, col_prev):
    n_dp = lax.axis_size("dp")
    d = lax.axis_index("dp")
    rows = tokens.shape[1]
    half = rows // n_dp
    widths = [half // 8] * 8

    def rows_part(start, width):
        return lax.dot_general(
            lax.dynamic_slice_in_dim(tokens, start, width, axis=1), cotangent,
            (((0,), (0,)), ((), ())), preferred_element_type=jnp.float32,
        ) * lax.dynamic_slice_in_dim(norm_gain, start, width)[:, None]

    pieces = []
    sums = []
    offset = 0
    for width in widths:
        send = rows_part((1 - d) * half + offset, width)
        if len(sums) >= LAG:
            send, _ = lax.optimization_barrier((send, sums[-LAG]))
        own = rows_part(d * half + offset, width)
        sums.append(own + lax.ppermute(send, "dp", SWAP))
        pieces.append(sums[-1] + lax.ppermute(sums[-1], "cuts", SWAP))
        offset += width
    gradient = jnp.concatenate(pieces, axis=0)

    squares = gradient * gradient
    col_sum = butterfly(butterfly(jnp.sum(squares, axis=0), "row"), "dp")
    col_moment = decay_rate * col_prev + (1.0 - decay_rate) * (col_sum / D + epsilon_one)
    weighted = jnp.sum(squares * (1.0 / col_moment)[None, :], axis=1)
    both = butterfly(jnp.stack([jnp.sum(squares, axis=1), weighted]), "col")
    row_moment = decay_rate * row_prev[0] + (1.0 - decay_rate) * (both[0] / F + epsilon_one)
    total_squares = jnp.sum(both[1] / row_moment)
    for axis in ("row", "dp"):
        total_squares = butterfly(total_squares, axis)
    clip_scale = jnp.maximum(1.0, jnp.sqrt(total_squares / (D * F)) / clip_level)
    factor = row_moment[:, None] * col_moment[None, :]
    raw_update = gradient / jnp.sqrt(factor)
    return ((raw_update / clip_scale)[None], row_moment[None], col_moment)


def solution(mesh):
    fast = mesh.shape["dp"] == 2 and mesh.shape["cuts"] == 2
    return jax.shard_map(
        body_swap if fast else body,
        mesh=mesh,
        in_specs=(
            P(("cuts", "dp"), "row"),
            P(("cuts", "dp"), "col"),
            P("row"),
            P("row", "dp"),
            P("col"),
        ),
        out_specs=(P("row", "dp", "col"), P("row", "dp"), P("col")),
        check_vma=False,
    )
```

```python
import jax
import jax.numpy as jnp
from jax import lax
from jax.sharding import PartitionSpec as P

D = 4096
F = 4096


decay_rate = 0.975
epsilon_one = 1e-30
clip_level = 1.0

SWAP = [(0, 1), (1, 0)]
LAG = 4


def gradient_rows(inputs, cotangent, gains):
    product = lax.dot_general(
        inputs, cotangent, (((0,), (0,)), ((), ())), preferred_element_type=jnp.float32
    )
    return product * gains[:, None]


def adafactor_step(gradient, rows_prev, cols_prev, down_columns, all_total):
    squares = gradient * gradient
    row_sum = lax.psum(jnp.sum(squares, axis=1), "col")
    col_sum = down_columns(jnp.sum(squares, axis=0))
    row_moment = decay_rate * rows_prev + (1.0 - decay_rate) * (row_sum / F + epsilon_one)
    col_moment = decay_rate * cols_prev + (1.0 - decay_rate) * (col_sum / D + epsilon_one)
    factor = row_moment[:, None] * col_moment[None, :]
    raw_update = gradient / jnp.sqrt(factor)
    total_squares = all_total(jnp.sum(raw_update * raw_update))
    clip_scale = jnp.maximum(1.0, jnp.sqrt(total_squares / (D * F)) / clip_level)
    return (raw_update / clip_scale, row_moment, col_moment)


def body(tokens, cotangent, norm_gain, row_prev, col_prev):
    slice_part = lax.psum_scatter(
        gradient_rows(tokens, cotangent, norm_gain), "dp", scatter_dimension=0, tiled=True
    )
    gradient = lax.psum(slice_part, "cuts")
    update, row_moment, col_moment = adafactor_step(
        gradient,
        row_prev[0],
        col_prev,
        lambda values: lax.psum(values, ("dp", "row")),
        lambda values: lax.psum(values, ("dp", "row", "col")),
    )
    return (update[None], row_moment[None], col_moment)


def butterfly(values, axis):
    step = 1
    while step < lax.axis_size(axis):
        pairs = [(i, i ^ step) for i in range(lax.axis_size(axis))]
        values = values + lax.ppermute(values, axis, pairs)
        step *= 2
    return values


def body_swap(tokens, cotangent, norm_gain, row_prev, col_prev):
    n_dp = lax.axis_size("dp")
    d = lax.axis_index("dp")
    rows = tokens.shape[1]
    half = rows // n_dp
    widths = [half // 8] * 8

    def rows_part(start, width):
        return lax.dot_general(
            lax.dynamic_slice_in_dim(tokens, start, width, axis=1), cotangent,
            (((0,), (0,)), ((), ())), preferred_element_type=jnp.float32,
        ) * lax.dynamic_slice_in_dim(norm_gain, start, width)[:, None]

    pieces = []
    sums = []
    offset = 0
    for width in widths:
        send = rows_part((1 - d) * half + offset, width)
        if len(sums) >= LAG:
            send, _ = lax.optimization_barrier((send, sums[-LAG]))
        own = rows_part(d * half + offset, width)
        sums.append(own + lax.ppermute(send, "dp", SWAP))
        pieces.append(sums[-1] + lax.ppermute(sums[-1], "cuts", SWAP))
        offset += width
    gradient = jnp.concatenate(pieces, axis=0)

    squares = gradient * gradient
    col_sum = butterfly(butterfly(jnp.sum(squares, axis=0), "row"), "dp")
    col_moment = decay_rate * col_prev + (1.0 - decay_rate) * (col_sum / D + epsilon_one)
    weighted = jnp.sum(squares * (1.0 / col_moment)[None, :], axis=1)
    both = butterfly(jnp.stack([jnp.sum(squares, axis=1), weighted]), "col")
    row_moment = decay_rate * row_prev[0] + (1.0 - decay_rate) * (both[0] / F + epsilon_one)
    total_squares = jnp.sum(both[1] / row_moment)
    for axis in ("row", "dp"):
        total_squares = butterfly(total_squares, axis)
    clip_scale = jnp.maximum(1.0, jnp.sqrt(total_squares / (D * F)) / clip_level)
    factor = row_moment[:, None] * col_moment[None, :]
    raw_update = gradient / jnp.sqrt(factor)
    return ((raw_update / clip_scale)[None], row_moment[None], col_moment)


def solution(mesh):
    fast = mesh.shape["dp"] == 2 and mesh.shape["cuts"] == 2
    return jax.shard_map(
        body_swap if fast else body,
        mesh=mesh,
        in_specs=(
            P(("cuts", "dp"), "row"),
            P(("cuts", "dp"), "col"),
            P("row"),
            P("row", "dp"),
            P("col"),
        ),
        out_specs=(P("row", "dp", "col"), P("row", "dp"), P("col")),
        check_vma=False,
    )
```

```python
import jax
import jax.numpy as jnp
from jax import lax
from jax.sharding import PartitionSpec as P

D = 4096
F = 4096


decay_rate = 0.975
epsilon_one = 1e-30
clip_level = 1.0

SWAP = [(0, 1), (1, 0)]
LAG = 3


def gradient_rows(inputs, cotangent, gains):
    product = lax.dot_general(
        inputs, cotangent, (((0,), (0,)), ((), ())), preferred_element_type=jnp.float32
    )
    return product * gains[:, None]


def adafactor_step(gradient, rows_prev, cols_prev, down_columns, all_total):
    squares = gradient * gradient
    row_sum = lax.psum(jnp.sum(squares, axis=1), "col")
    col_sum = down_columns(jnp.sum(squares, axis=0))
    row_moment = decay_rate * rows_prev + (1.0 - decay_rate) * (row_sum / F + epsilon_one)
    col_moment = decay_rate * cols_prev + (1.0 - decay_rate) * (col_sum / D + epsilon_one)
    factor = row_moment[:, None] * col_moment[None, :]
    raw_update = gradient / jnp.sqrt(factor)
    total_squares = all_total(jnp.sum(raw_update * raw_update))
    clip_scale = jnp.maximum(1.0, jnp.sqrt(total_squares / (D * F)) / clip_level)
    return (raw_update / clip_scale, row_moment, col_moment)


def body(tokens, cotangent, norm_gain, row_prev, col_prev):
    slice_part = lax.psum_scatter(
        gradient_rows(tokens, cotangent, norm_gain), "dp", scatter_dimension=0, tiled=True
    )
    gradient = lax.psum(slice_part, "cuts")
    update, row_moment, col_moment = adafactor_step(
        gradient,
        row_prev[0],
        col_prev,
        lambda values: lax.psum(values, ("dp", "row")),
        lambda values: lax.psum(values, ("dp", "row", "col")),
    )
    return (update[None], row_moment[None], col_moment)


def butterfly(values, axis):
    step = 1
    while step < lax.axis_size(axis):
        pairs = [(i, i ^ step) for i in range(lax.axis_size(axis))]
        values = values + lax.ppermute(values, axis, pairs)
        step *= 2
    return values


def body_swap(tokens, cotangent, norm_gain, row_prev, col_prev):
    n_dp = lax.axis_size("dp")
    d = lax.axis_index("dp")
    rows = tokens.shape[1]
    half = rows // n_dp
    unit = half // 32
    widths = [unit, unit * 3] + [unit * 4] * 7

    def rows_part(start, width):
        return lax.dot_general(
            lax.dynamic_slice_in_dim(tokens, start, width, axis=1), cotangent,
            (((0,), (0,)), ((), ())), preferred_element_type=jnp.float32,
        ) * lax.dynamic_slice_in_dim(norm_gain, start, width)[:, None]

    pieces = []
    sums = []
    offset = 0
    for width in widths:
        send = rows_part((1 - d) * half + offset, width)
        if len(sums) >= LAG:
            send, _ = lax.optimization_barrier((send, sums[-LAG]))
        own = rows_part(d * half + offset, width)
        sums.append(own + lax.ppermute(send, "dp", SWAP))
        pieces.append(sums[-1] + lax.ppermute(sums[-1], "cuts", SWAP))
        offset += width
    gradient = jnp.concatenate(pieces, axis=0)

    squares = gradient * gradient
    col_sum = butterfly(butterfly(jnp.sum(squares, axis=0), "row"), "dp")
    col_moment = decay_rate * col_prev + (1.0 - decay_rate) * (col_sum / D + epsilon_one)
    weighted = jnp.sum(squares * (1.0 / col_moment)[None, :], axis=1)
    both = butterfly(jnp.stack([jnp.sum(squares, axis=1), weighted]), "col")
    row_moment = decay_rate * row_prev[0] + (1.0 - decay_rate) * (both[0] / F + epsilon_one)
    total_squares = jnp.sum(both[1] / row_moment)
    for axis in ("row", "dp"):
        total_squares = butterfly(total_squares, axis)
    clip_scale = jnp.maximum(1.0, jnp.sqrt(total_squares / (D * F)) / clip_level)
    factor = row_moment[:, None] * col_moment[None, :]
    raw_update = gradient / jnp.sqrt(factor)
    return ((raw_update / clip_scale)[None], row_moment[None], col_moment)


def solution(mesh):
    fast = mesh.shape["dp"] == 2 and mesh.shape["cuts"] == 2
    return jax.shard_map(
        body_swap if fast else body,
        mesh=mesh,
        in_specs=(
            P(("cuts", "dp"), "row"),
            P(("cuts", "dp"), "col"),
            P("row"),
            P("row", "dp"),
            P("col"),
        ),
        out_specs=(P("row", "dp", "col"), P("row", "dp"), P("col")),
        check_vma=False,
    )
```

```python
import jax
import jax.numpy as jnp
from jax import lax
from jax.sharding import PartitionSpec as P

D = 4096
F = 4096


decay_rate = 0.975
epsilon_one = 1e-30
clip_level = 1.0

SWAP = [(0, 1), (1, 0)]
LAG = 3


def gradient_rows(inputs, cotangent, gains):
    product = lax.dot_general(
        inputs, cotangent, (((0,), (0,)), ((), ())), preferred_element_type=jnp.float32
    )
    return product * gains[:, None]


def adafactor_step(gradient, rows_prev, cols_prev, down_columns, all_total):
    squares = gradient * gradient
    row_sum = lax.psum(jnp.sum(squares, axis=1), "col")
    col_sum = down_columns(jnp.sum(squares, axis=0))
    row_moment = decay_rate * rows_prev + (1.0 - decay_rate) * (row_sum / F + epsilon_one)
    col_moment = decay_rate * cols_prev + (1.0 - decay_rate) * (col_sum / D + epsilon_one)
    factor = row_moment[:, None] * col_moment[None, :]
    raw_update = gradient / jnp.sqrt(factor)
    total_squares = all_total(jnp.sum(raw_update * raw_update))
    clip_scale = jnp.maximum(1.0, jnp.sqrt(total_squares / (D * F)) / clip_level)
    return (raw_update / clip_scale, row_moment, col_moment)


def body(tokens, cotangent, norm_gain, row_prev, col_prev):
    slice_part = lax.psum_scatter(
        gradient_rows(tokens, cotangent, norm_gain), "dp", scatter_dimension=0, tiled=True
    )
    gradient = lax.psum(slice_part, "cuts")
    update, row_moment, col_moment = adafactor_step(
        gradient,
        row_prev[0],
        col_prev,
        lambda values: lax.psum(values, ("dp", "row")),
        lambda values: lax.psum(values, ("dp", "row", "col")),
    )
    return (update[None], row_moment[None], col_moment)


def butterfly(values, axis):
    step = 1
    while step < lax.axis_size(axis):
        pairs = [(i, i ^ step) for i in range(lax.axis_size(axis))]
        values = values + lax.ppermute(values, axis, pairs)
        step *= 2
    return values


def body_swap(tokens, cotangent, norm_gain, row_prev, col_prev):
    n_dp = lax.axis_size("dp")
    d = lax.axis_index("dp")
    rows = tokens.shape[1]
    half = rows // n_dp
    unit = half // 32
    widths = [unit * 2] * 2 + [unit * 4] * 6 + [unit * 2] * 2

    def rows_part(start, width):
        return lax.dot_general(
            lax.dynamic_slice_in_dim(tokens, start, width, axis=1), cotangent,
            (((0,), (0,)), ((), ())), preferred_element_type=jnp.float32,
        ) * lax.dynamic_slice_in_dim(norm_gain, start, width)[:, None]

    pieces = []
    sums = []
    offset = 0
    for width in widths:
        send = rows_part((1 - d) * half + offset, width)
        if len(sums) >= LAG:
            send, _ = lax.optimization_barrier((send, sums[-LAG]))
        own = rows_part(d * half + offset, width)
        sums.append(own + lax.ppermute(send, "dp", SWAP))
        pieces.append(sums[-1] + lax.ppermute(sums[-1], "cuts", SWAP))
        offset += width
    gradient = jnp.concatenate(pieces, axis=0)

    squares = gradient * gradient
    col_sum = butterfly(butterfly(jnp.sum(squares, axis=0), "row"), "dp")
    col_moment = decay_rate * col_prev + (1.0 - decay_rate) * (col_sum / D + epsilon_one)
    weighted = jnp.sum(squares * (1.0 / col_moment)[None, :], axis=1)
    both = butterfly(jnp.stack([jnp.sum(squares, axis=1), weighted]), "col")
    row_moment = decay_rate * row_prev[0] + (1.0 - decay_rate) * (both[0] / F + epsilon_one)
    total_squares = jnp.sum(both[1] / row_moment)
    for axis in ("row", "dp"):
        total_squares = butterfly(total_squares, axis)
    clip_scale = jnp.maximum(1.0, jnp.sqrt(total_squares / (D * F)) / clip_level)
    factor = row_moment[:, None] * col_moment[None, :]
    raw_update = gradient / jnp.sqrt(factor)
    return ((raw_update / clip_scale)[None], row_moment[None], col_moment)


def solution(mesh):
    fast = mesh.shape["dp"] == 2 and mesh.shape["cuts"] == 2
    return jax.shard_map(
        body_swap if fast else body,
        mesh=mesh,
        in_specs=(
            P(("cuts", "dp"), "row"),
            P(("cuts", "dp"), "col"),
            P("row"),
            P("row", "dp"),
            P("col"),
        ),
        out_specs=(P("row", "dp", "col"), P("row", "dp"), P("col")),
        check_vma=False,
    )
```

```python
import jax
import jax.numpy as jnp
from jax import lax
from jax.sharding import PartitionSpec as P

D = 4096
F = 4096


decay_rate = 0.975
epsilon_one = 1e-30
clip_level = 1.0

SWAP = [(0, 1), (1, 0)]
LAG = 3


def gradient_rows(inputs, cotangent, gains):
    product = lax.dot_general(
        inputs, cotangent, (((0,), (0,)), ((), ())), preferred_element_type=jnp.float32
    )
    return product * gains[:, None]


def adafactor_step(gradient, rows_prev, cols_prev, down_columns, all_total):
    squares = gradient * gradient
    row_sum = lax.psum(jnp.sum(squares, axis=1), "col")
    col_sum = down_columns(jnp.sum(squares, axis=0))
    row_moment = decay_rate * rows_prev + (1.0 - decay_rate) * (row_sum / F + epsilon_one)
    col_moment = decay_rate * cols_prev + (1.0 - decay_rate) * (col_sum / D + epsilon_one)
    factor = row_moment[:, None] * col_moment[None, :]
    raw_update = gradient / jnp.sqrt(factor)
    total_squares = all_total(jnp.sum(raw_update * raw_update))
    clip_scale = jnp.maximum(1.0, jnp.sqrt(total_squares / (D * F)) / clip_level)
    return (raw_update / clip_scale, row_moment, col_moment)


def body(tokens, cotangent, norm_gain, row_prev, col_prev):
    slice_part = lax.psum_scatter(
        gradient_rows(tokens, cotangent, norm_gain), "dp", scatter_dimension=0, tiled=True
    )
    gradient = lax.psum(slice_part, "cuts")
    update, row_moment, col_moment = adafactor_step(
        gradient,
        row_prev[0],
        col_prev,
        lambda values: lax.psum(values, ("dp", "row")),
        lambda values: lax.psum(values, ("dp", "row", "col")),
    )
    return (update[None], row_moment[None], col_moment)


def butterfly(values, axis):
    step = 1
    while step < lax.axis_size(axis):
        pairs = [(i, i ^ step) for i in range(lax.axis_size(axis))]
        values = values + lax.ppermute(values, axis, pairs)
        step *= 2
    return values


def body_swap(tokens, cotangent, norm_gain, row_prev, col_prev):
    n_dp = lax.axis_size("dp")
    d = lax.axis_index("dp")
    rows = tokens.shape[1]
    half = rows // n_dp
    widths = [half // 8] * 8

    def rows_part(start, width):
        return lax.dot_general(
            lax.dynamic_slice_in_dim(tokens, start, width, axis=1), cotangent,
            (((0,), (0,)), ((), ())), preferred_element_type=jnp.float32,
        ) * lax.dynamic_slice_in_dim(norm_gain, start, width)[:, None]

    c_idx = lax.axis_index("cuts")
    quarter = widths[0] // 2
    first_own = rows_part(d * half, widths[0])
    first_send = rows_part((1 - d) * half, widths[0])
    kept = lambda x: lax.dynamic_slice_in_dim(x, c_idx * quarter, quarter)
    given = lambda x: lax.dynamic_slice_in_dim(x, (1 - c_idx) * quarter, quarter)
    across = lax.ppermute(
        jnp.concatenate([given(first_own), given(first_send)]), "cuts", SWAP
    )
    slab_send = kept(first_send) + across[quarter:]
    slab = kept(first_own) + across[:quarter] + lax.ppermute(slab_send, "dp", SWAP)
    other = lax.ppermute(slab, "cuts", SWAP)
    pieces = [jnp.where(c_idx == 0, jnp.concatenate([slab, other]), jnp.concatenate([other, slab]))]
    sums = [slab]
    offset = widths[0]
    for width in widths[1:]:
        send = rows_part((1 - d) * half + offset, width)
        if len(sums) >= LAG:
            send, _ = lax.optimization_barrier((send, sums[-LAG]))
        own = rows_part(d * half + offset, width)
        sums.append(own + lax.ppermute(send, "dp", SWAP))
        pieces.append(sums[-1] + lax.ppermute(sums[-1], "cuts", SWAP))
        offset += width
    gradient = jnp.concatenate(pieces, axis=0)

    squares = gradient * gradient
    col_sum = butterfly(butterfly(jnp.sum(squares, axis=0), "row"), "dp")
    col_moment = decay_rate * col_prev + (1.0 - decay_rate) * (col_sum / D + epsilon_one)
    weighted = jnp.sum(squares * (1.0 / col_moment)[None, :], axis=1)
    both = butterfly(jnp.stack([jnp.sum(squares, axis=1), weighted]), "col")
    row_moment = decay_rate * row_prev[0] + (1.0 - decay_rate) * (both[0] / F + epsilon_one)
    total_squares = jnp.sum(both[1] / row_moment)
    for axis in ("row", "dp"):
        total_squares = butterfly(total_squares, axis)
    clip_scale = jnp.maximum(1.0, jnp.sqrt(total_squares / (D * F)) / clip_level)
    factor = row_moment[:, None] * col_moment[None, :]
    raw_update = gradient / jnp.sqrt(factor)
    return ((raw_update / clip_scale)[None], row_moment[None], col_moment)


def solution(mesh):
    fast = mesh.shape["dp"] == 2 and mesh.shape["cuts"] == 2
    return jax.shard_map(
        body_swap if fast else body,
        mesh=mesh,
        in_specs=(
            P(("cuts", "dp"), "row"),
            P(("cuts", "dp"), "col"),
            P("row"),
            P("row", "dp"),
            P("col"),
        ),
        out_specs=(P("row", "dp", "col"), P("row", "dp"), P("col")),
        check_vma=False,
    )
```

```python
import jax
import jax.numpy as jnp
from jax import lax
from jax.sharding import PartitionSpec as P

D = 4096
F = 4096


decay_rate = 0.975
epsilon_one = 1e-30
clip_level = 1.0

SWAP = [(0, 1), (1, 0)]
LAG = 3


def gradient_rows(inputs, cotangent, gains):
    product = lax.dot_general(
        inputs, cotangent, (((0,), (0,)), ((), ())), preferred_element_type=jnp.float32
    )
    return product * gains[:, None]


def adafactor_step(gradient, rows_prev, cols_prev, down_columns, all_total):
    squares = gradient * gradient
    row_sum = lax.psum(jnp.sum(squares, axis=1), "col")
    col_sum = down_columns(jnp.sum(squares, axis=0))
    row_moment = decay_rate * rows_prev + (1.0 - decay_rate) * (row_sum / F + epsilon_one)
    col_moment = decay_rate * cols_prev + (1.0 - decay_rate) * (col_sum / D + epsilon_one)
    factor = row_moment[:, None] * col_moment[None, :]
    raw_update = gradient / jnp.sqrt(factor)
    total_squares = all_total(jnp.sum(raw_update * raw_update))
    clip_scale = jnp.maximum(1.0, jnp.sqrt(total_squares / (D * F)) / clip_level)
    return (raw_update / clip_scale, row_moment, col_moment)


def body(tokens, cotangent, norm_gain, row_prev, col_prev):
    slice_part = lax.psum_scatter(
        gradient_rows(tokens, cotangent, norm_gain), "dp", scatter_dimension=0, tiled=True
    )
    gradient = lax.psum(slice_part, "cuts")
    update, row_moment, col_moment = adafactor_step(
        gradient,
        row_prev[0],
        col_prev,
        lambda values: lax.psum(values, ("dp", "row")),
        lambda values: lax.psum(values, ("dp", "row", "col")),
    )
    return (update[None], row_moment[None], col_moment)


def butterfly(values, axis):
    step = 1
    while step < lax.axis_size(axis):
        pairs = [(i, i ^ step) for i in range(lax.axis_size(axis))]
        values = values + lax.ppermute(values, axis, pairs)
        step *= 2
    return values


def body_swap(tokens, cotangent, norm_gain, row_prev, col_prev):
    n_dp = lax.axis_size("dp")
    d = lax.axis_index("dp")
    rows = tokens.shape[1]
    half = rows // n_dp
    widths = [half // 8] * 8

    def rows_part(start, width):
        return lax.dot_general(
            lax.dynamic_slice_in_dim(tokens, start, width, axis=1), cotangent,
            (((0,), (0,)), ((), ())), preferred_element_type=jnp.float32,
        ) * lax.dynamic_slice_in_dim(norm_gain, start, width)[:, None]

    pieces = []
    sums = []
    offset = 0
    for width in widths:
        send = rows_part((1 - d) * half + offset, width)
        if len(sums) >= LAG:
            send, _ = lax.optimization_barrier((send, sums[-LAG]))
        own = rows_part(d * half + offset, width)
        sums.append(own + lax.ppermute(send, "dp", SWAP))
        pieces.append(sums[-1] + lax.ppermute(sums[-1], "cuts", SWAP))
        offset += width
    gradient = jnp.concatenate(pieces, axis=0)

    squares = gradient * gradient
    col_sum = butterfly(butterfly(jnp.sum(squares, axis=0), "row"), "dp")
    col_moment = decay_rate * col_prev + (1.0 - decay_rate) * (col_sum / D + epsilon_one)
    weighted = jnp.sum(squares * (1.0 / col_moment)[None, :], axis=1)
    both = butterfly(jnp.stack([jnp.sum(squares, axis=1), weighted]), "col")
    row_moment = decay_rate * row_prev[0] + (1.0 - decay_rate) * (both[0] / F + epsilon_one)
    total_squares = jnp.sum(both[1] / row_moment)
    for axis in ("row", "dp"):
        total_squares = butterfly(total_squares, axis)
    clip_scale = jnp.maximum(1.0, jnp.sqrt(total_squares / (D * F)) / clip_level)
    row_scale = 1.0 / (jnp.sqrt(row_moment) * clip_scale)
    col_scale = 1.0 / jnp.sqrt(col_moment)
    update = gradient * row_scale[:, None] * col_scale[None, :]
    return (update[None], row_moment[None], col_moment)


def solution(mesh):
    fast = mesh.shape["dp"] == 2 and mesh.shape["cuts"] == 2
    return jax.shard_map(
        body_swap if fast else body,
        mesh=mesh,
        in_specs=(
            P(("cuts", "dp"), "row"),
            P(("cuts", "dp"), "col"),
            P("row"),
            P("row", "dp"),
            P("col"),
        ),
        out_specs=(P("row", "dp", "col"), P("row", "dp"), P("col")),
        check_vma=False,
    )
```

```python
import jax
import jax.numpy as jnp
from jax import lax
from jax.sharding import PartitionSpec as P

D = 4096
F = 4096


decay_rate = 0.975
epsilon_one = 1e-30
clip_level = 1.0

SWAP = [(0, 1), (1, 0)]
LAG = 3


def gradient_rows(inputs, cotangent, gains):
    product = lax.dot_general(
        inputs, cotangent, (((0,), (0,)), ((), ())), preferred_element_type=jnp.float32
    )
    return product * gains[:, None]


def adafactor_step(gradient, rows_prev, cols_prev, down_columns, all_total):
    squares = gradient * gradient
    row_sum = lax.psum(jnp.sum(squares, axis=1), "col")
    col_sum = down_columns(jnp.sum(squares, axis=0))
    row_moment = decay_rate * rows_prev + (1.0 - decay_rate) * (row_sum / F + epsilon_one)
    col_moment = decay_rate * cols_prev + (1.0 - decay_rate) * (col_sum / D + epsilon_one)
    factor = row_moment[:, None] * col_moment[None, :]
    raw_update = gradient / jnp.sqrt(factor)
    total_squares = all_total(jnp.sum(raw_update * raw_update))
    clip_scale = jnp.maximum(1.0, jnp.sqrt(total_squares / (D * F)) / clip_level)
    return (raw_update / clip_scale, row_moment, col_moment)


def body(tokens, cotangent, norm_gain, row_prev, col_prev):
    slice_part = lax.psum_scatter(
        gradient_rows(tokens, cotangent, norm_gain), "dp", scatter_dimension=0, tiled=True
    )
    gradient = lax.psum(slice_part, "cuts")
    update, row_moment, col_moment = adafactor_step(
        gradient,
        row_prev[0],
        col_prev,
        lambda values: lax.psum(values, ("dp", "row")),
        lambda values: lax.psum(values, ("dp", "row", "col")),
    )
    return (update[None], row_moment[None], col_moment)


def butterfly(values, axis):
    step = 1
    while step < lax.axis_size(axis):
        pairs = [(i, i ^ step) for i in range(lax.axis_size(axis))]
        values = values + lax.ppermute(values, axis, pairs)
        step *= 2
    return values


def body_swap(tokens, cotangent, norm_gain, row_prev, col_prev):
    n_dp = lax.axis_size("dp")
    d = lax.axis_index("dp")
    rows = tokens.shape[1]
    half = rows // n_dp
    widths = [half // 8] * 8

    def rows_part(start, width):
        return lax.dot_general(
            lax.dynamic_slice_in_dim(tokens, start, width, axis=1), cotangent,
            (((0,), (0,)), ((), ())), preferred_element_type=jnp.float32,
        ) * lax.dynamic_slice_in_dim(norm_gain, start, width)[:, None]

    pieces = []
    sums = []
    offset = 0
    for width in widths:
        send = rows_part((1 - d) * half + offset, width)
        if len(sums) >= LAG:
            send, _ = lax.optimization_barrier((send, sums[-LAG]))
        own = rows_part(d * half + offset, width)
        sums.append(own + lax.ppermute(send, "dp", SWAP))
        split = width // 2
        pieces.append(sums[-1][:split] + lax.ppermute(sums[-1][:split], "cuts", SWAP))
        pieces.append(sums[-1][split:] + lax.ppermute(sums[-1][split:], "cuts", SWAP))
        offset += width
    gradient = jnp.concatenate(pieces, axis=0)

    squares = gradient * gradient
    col_sum = butterfly(butterfly(jnp.sum(squares, axis=0), "row"), "dp")
    col_moment = decay_rate * col_prev + (1.0 - decay_rate) * (col_sum / D + epsilon_one)
    weighted = jnp.sum(squares * (1.0 / col_moment)[None, :], axis=1)
    both = butterfly(jnp.stack([jnp.sum(squares, axis=1), weighted]), "col")
    row_moment = decay_rate * row_prev[0] + (1.0 - decay_rate) * (both[0] / F + epsilon_one)
    total_squares = jnp.sum(both[1] / row_moment)
    for axis in ("row", "dp"):
        total_squares = butterfly(total_squares, axis)
    clip_scale = jnp.maximum(1.0, jnp.sqrt(total_squares / (D * F)) / clip_level)
    factor = row_moment[:, None] * col_moment[None, :]
    raw_update = gradient / jnp.sqrt(factor)
    return ((raw_update / clip_scale)[None], row_moment[None], col_moment)


def solution(mesh):
    fast = mesh.shape["dp"] == 2 and mesh.shape["cuts"] == 2
    return jax.shard_map(
        body_swap if fast else body,
        mesh=mesh,
        in_specs=(
            P(("cuts", "dp"), "row"),
            P(("cuts", "dp"), "col"),
            P("row"),
            P("row", "dp"),
            P("col"),
        ),
        out_specs=(P("row", "dp", "col"), P("row", "dp"), P("col")),
        check_vma=False,
    )
```
